512 devices in a mesh: frame: 8 (over y_lo, core), space: 64 (over x, y_hi, z).
Axes of the slice: x: 4, y: 8 (y_hi: 2, y_lo: 4; y = y_hi * 4 + y_lo), z: 8, core: 2. Of those that a mesh axis runs over, the one named last changes fastest.
Arguments:
- queries: bfloat16 [8, 960, 8, 1024], P('frame', 'space'), may hold values from -38 to 38
- key_proj: bfloat16 [8, 960, 8, 1024], P('frame', 'space'), may hold values from -6 to 6
- value_proj: bfloat16 [8, 960, 8, 1024], P('frame', 'space'), may hold values from -6 to 6
- grad_out: bfloat16 [8, 960, 8, 1024], P('frame', 'space'), may hold values from -12 to 12
- gate_vec: float32 [8, 1024], replicated, may hold values from 0.3 to 3
Outputs:
- grad_query: bfloat16 [8, 960, 8, 1024], P('frame', 'space')
- grad_key: bfloat16 [8, 960, 8, 1024], P('frame', 'space')
- grad_value: bfloat16 [8, 960, 8, 1024], P('frame', 'space')
- grad_gate: float32 [64, 128], P('space')
The draws below stay inside these ranges and needn't reach their ends.
All inputs are finite; a program needn't handle non-finite values.
Results may differ from the reference program's by a relative error of at most 0.024.
Values may be sent and summed in bfloat16 or wider, within the bound.
No kernel may reach another device: no remote copies, remote signals or barrier semaphores. Data moves between devices by JAX's collectives and lax.ppermute only.
A program may use at most 64 MiB of HBM per device.

```python
import math
import jax
import jax.numpy as jnp
from jax import lax

DH = 128
HEADS = 8
WIDTH = 1024
PIXELS = 960
CLIPS = 8
FRAMES = 8


def paired_draw(key):
    full_shape = (FRAMES, PIXELS, CLIPS, HEADS * DH)
    query_seed = jax.random.fold_in(key, 11)
    key_seed = jax.random.fold_in(key, 23)
    key_rows = jnp.clip(1.25 * jax.random.normal(key_seed, full_shape, jnp.float32), -5.0, 5.0)
    query_rows = jnp.clip(1.25 * jax.random.normal(query_seed, full_shape, jnp.float32), -5.0, 5.0)
    return (query_rows, key_rows)


def draw_queries(key, part):
    return paired_draw(key)[0].astype(jnp.bfloat16)


def draw_key_proj(key, part):
    return paired_draw(key)[1].astype(jnp.bfloat16)


def block_levels(rng, dims, split, low, largest):
    def one(dim, shards_of):
        steps = jax.random.uniform(jax.random.fold_in(jax.random.fold_in(rng, 6), dim), (shards_of,), jnp.float32, low / len(split), largest / len(split))
        return jnp.repeat(jnp.exp(steps), dims[dim] // shards_of).reshape((-1,) + (1,) * (len(dims) - dim - 1))

    loudness = one(*split[0])
    for cut in split[1:]:
        loudness = loudness * one(*cut)
    return loudness


def bell_draw(rng, shape, width, limit, cuts=(), held_as=jnp.bfloat16):
    factor_of = block_levels(rng, shape, cuts, -0.22, 0.18) if cuts else 1.0
    values = jax.random.normal(rng, shape, jnp.float32) * width * factor_of
    return jnp.minimum(jnp.maximum(values, -limit), limit).astype(held_as)


def setup_inputs(seed: int = 0) -> dict:
    key_of = jax.random.split(jax.random.key(seed), 6)
    queries = draw_queries(jax.random.fold_in(key_of[5], 71), 0)
    key_proj = draw_key_proj(jax.random.fold_in(key_of[5], 71), 0)
    value_proj = bell_draw(key_of[2], (FRAMES, PIXELS, CLIPS, WIDTH), 1.0, 6.0, ((0, 8), (1, 64)))
    grad_out = bell_draw(key_of[3], (FRAMES, PIXELS, CLIPS, WIDTH), 2.0, 12.0, ((0, 8), (1, 64)))
    gate_vec = jnp.clip(jnp.exp(jax.random.uniform(key_of[4], (CLIPS, WIDTH), jnp.float32, math.log(0.3), math.log(3.0))), 0.3, 3.0)
    return {"queries": queries, "key_proj": key_proj, "value_proj": value_proj, "grad_out": grad_out, "gate_vec": gate_vec}


def item_grads(operands):
    query_one, key_one, value_one, upstream, gate_row = operands
    inv_root = 1.0 / math.sqrt(DH)
    scores = jnp.dot(query_one, key_one.T, preferred_element_type=jnp.float32) * inv_root
    row_peak = lax.optimization_barrier(jnp.max(scores, axis=-1, keepdims=True))
    exp_terms = jnp.exp(scores - row_peak)
    attention = exp_terms / lax.optimization_barrier(jnp.sum(exp_terms, axis=-1, keepdims=True))
    attention_low = attention.astype(jnp.bfloat16)
    attended = jnp.dot(attention_low, value_one, preferred_element_type=jnp.float32)
    upstream_wide = upstream.astype(jnp.float32)
    cotangent = (gate_row[None, :] * upstream_wide).astype(jnp.bfloat16)
    gate_part = lax.optimization_barrier(jnp.sum(upstream_wide * attended, axis=0))
    grad_attn = jnp.dot(cotangent, value_one.T, preferred_element_type=jnp.float32)
    row_terms = lax.optimization_barrier(jnp.sum(cotangent.astype(jnp.float32) * attended, axis=-1, keepdims=True))
    grad_scores = (attention * (grad_attn - row_terms)).astype(jnp.bfloat16)
    grad_query = (jnp.dot(grad_scores, key_one, preferred_element_type=jnp.float32) * inv_root).astype(jnp.bfloat16)
    grad_key = (jnp.dot(grad_scores.T, query_one, preferred_element_type=jnp.float32) * inv_root).astype(jnp.bfloat16)
    grad_value = jnp.dot(attention_low.T, cotangent, preferred_element_type=jnp.float32).astype(jnp.bfloat16)
    return (grad_query, grad_key, grad_value, gate_part)

def to_items(tensor):
    shaped = tensor.reshape(FRAMES, PIXELS, CLIPS, HEADS, DH)
    return jnp.transpose(shaped, (0, 2, 3, 1, 4)).reshape(FRAMES * CLIPS * HEADS, PIXELS, DH)

def from_items(tensor):
    shaped = tensor.reshape(FRAMES, CLIPS, HEADS, PIXELS, DH)
    return jnp.transpose(shaped, (0, 3, 1, 2, 4)).reshape(FRAMES, PIXELS, CLIPS, HEADS * DH)

def reference(queries, key_proj, value_proj, grad_out, gate_vec):
    gate_items = jnp.broadcast_to(gate_vec.reshape(1, CLIPS, HEADS, DH), (FRAMES, CLIPS, HEADS, DH))
    gate_items = gate_items.reshape(FRAMES * CLIPS * HEADS, DH)
    results = lax.map(item_grads, (to_items(queries), to_items(key_proj), to_items(value_proj), to_items(grad_out), gate_items))
    grad_query, grad_key, grad_value, gate_parts = results
    grad_gate = lax.optimization_barrier(jnp.sum(gate_parts.reshape(FRAMES, CLIPS * HEADS, DH), axis=0))
    return (from_items(grad_query), from_items(grad_key), from_items(grad_value), grad_gate)
```

```python
import math

import jax
import jax.numpy as jnp
from jax import lax
from jax.sharding import PartitionSpec as P

DH = 128


def shortened(value):

    def short(part):
        return part.astype(jnp.bfloat16) if part.dtype == jnp.float32 else part

    return jax.tree.map(short, value)


def item_grads(query_one, key_one, value_one, upstream, gate_row):
    channels = query_one.shape[1]
    inv_root = 1.0 / math.sqrt(channels)
    scores = jnp.dot(query_one, key_one.T, preferred_element_type=jnp.float32) * inv_root
    row_peak = jnp.max(scores, axis=-1, keepdims=True)
    exp_terms = jnp.exp(scores - row_peak)
    attention = exp_terms / jnp.sum(exp_terms, axis=-1, keepdims=True)
    attention_low = attention.astype(jnp.bfloat16)
    attended_blk = jnp.dot(attention_low, value_one, preferred_element_type=jnp.float32)
    upstream_wide = upstream.astype(jnp.float32)
    cotangent = (gate_row[None, :] * upstream_wide).astype(jnp.bfloat16)
    gate_part = jnp.sum(upstream_wide * attended_blk, axis=0)
    grad_attn = jnp.dot(cotangent, value_one.T, preferred_element_type=jnp.float32)
    row_terms = jnp.sum(cotangent.astype(jnp.float32) * attended_blk, axis=-1, keepdims=True)
    grad_scores = (attention * (grad_attn - row_terms)).astype(jnp.bfloat16)
    query_parts = [
        (jnp.dot(grad_scores, key_one, preferred_element_type=jnp.float32) * inv_root).astype(
            jnp.bfloat16
        )
    ]
    attended_parts = [attended_blk]
    key_acc = jnp.dot(grad_scores.T, query_one, preferred_element_type=jnp.float32)
    value_acc = jnp.dot(attention_low.T, cotangent, preferred_element_type=jnp.float32)
    grad_query = jnp.concatenate(query_parts, axis=0)
    grad_key = (key_acc * inv_root).astype(jnp.bfloat16)
    grad_value = value_acc.astype(jnp.bfloat16)
    attended = jnp.concatenate(attended_parts, axis=0)
    return (grad_query, grad_key, grad_value, attended, gate_part)


def local(queries, key_proj, value_proj, grad_out, gate_vec):
    frames_local, pixels_local, clip_count, channels = queries.shape
    head_count = channels // DH
    pair_count = clip_count * head_count

    def by_pair(tensor):
        return tensor.reshape(frames_local, pixels_local, pair_count, DH)

    def by_width(tensor):
        return tensor.reshape(frames_local, pixels_local, clip_count, channels)

    stacked = jnp.stack(
        [by_pair(queries), by_pair(key_proj), by_pair(value_proj), by_pair(grad_out)], axis=0
    )
    gathered = lax.all_to_all(stacked, "space", split_axis=3, concat_axis=2, tiled=True)
    query_all, key_all, value_all, upstream_all = (
        gathered[0], gathered[1], gathered[2], gathered[3]
    )
    pairs_local = query_all.shape[2]
    gate_rows = lax.dynamic_slice_in_dim(
        gate_vec.reshape(pair_count, DH), lax.axis_index("space") * pairs_local, pairs_local, 0
    )
    per_pair = jax.vmap(item_grads, in_axes=(1, 1, 1, 1, 0), out_axes=(1, 1, 1, 1, 0))
    per_frame = jax.vmap(per_pair, in_axes=(0, 0, 0, 0, None), out_axes=0)
    grad_query, grad_key, grad_value, attended, gate_parts = per_frame(
        query_all, key_all, value_all, upstream_all, gate_rows
    )
    grads = jnp.stack([grad_query, grad_key, grad_value], axis=0)
    back = lax.all_to_all(grads, "space", split_axis=2, concat_axis=3, tiled=True)
    back_query, back_key, back_value = back[0], back[1], back[2]
    pair_terms = jnp.sum(gate_parts, axis=0)
    grad_gate = lax.psum(pair_terms, "frame")
    return (by_width(back_query), by_width(back_key), by_width(back_value), grad_gate)


def solution(mesh):
    in_specs = (
        P("frame", "space", None, None),
        P("frame", "space", None, None),
        P("frame", "space", None, None),
        P("frame", "space", None, None),
        P(),
    )
    out_specs = (
        P("frame", "space", None, None),
        P("frame", "space", None, None),
        P("frame", "space", None, None),
        P("space", None),
    )
    return jax.shard_map(local, mesh=mesh, in_specs=in_specs, out_specs=out_specs, check_vma=False)
```

```python
import math

import jax
import jax.numpy as jnp
from jax import lax
from jax.sharding import PartitionSpec as P

DH = 128


def shortened(value):

    def short(part):
        return part.astype(jnp.bfloat16) if part.dtype == jnp.float32 else part

    return jax.tree.map(short, value)


def item_grads(query_one, key_one, value_one, upstream, gate_row):
    channels = query_one.shape[1]
    inv_root = 1.0 / math.sqrt(channels)
    scores = jnp.dot(query_one, key_one.T, preferred_element_type=jnp.float32) * inv_root
    row_peak = jnp.max(scores, axis=-1, keepdims=True)
    exp_terms = jnp.exp(scores - row_peak)
    attention = exp_terms / jnp.sum(exp_terms, axis=-1, keepdims=True)
    attention_low = attention.astype(jnp.bfloat16)
    attended_blk = jnp.dot(attention_low, value_one, preferred_element_type=jnp.float32)
    upstream_wide = upstream.astype(jnp.float32)
    cotangent = (gate_row[None, :] * upstream_wide).astype(jnp.bfloat16)
    gate_part = jnp.sum(upstream_wide * attended_blk, axis=0)
    grad_attn = jnp.dot(cotangent, value_one.T, preferred_element_type=jnp.float32)
    row_terms = jnp.sum(cotangent.astype(jnp.float32) * attended_blk, axis=-1, keepdims=True)
    grad_scores = (attention * (grad_attn - row_terms)).astype(jnp.bfloat16)
    query_parts = [
        (jnp.dot(grad_scores, key_one, preferred_element_type=jnp.float32) * inv_root).astype(
            jnp.bfloat16
        )
    ]
    attended_parts = [attended_blk]
    key_acc = jnp.dot(grad_scores.T, query_one, preferred_element_type=jnp.float32)
    value_acc = jnp.dot(attention_low.T, cotangent, preferred_element_type=jnp.float32)
    grad_query = jnp.concatenate(query_parts, axis=0)
    grad_key = (key_acc * inv_root).astype(jnp.bfloat16)
    grad_value = value_acc.astype(jnp.bfloat16)
    attended = jnp.concatenate(attended_parts, axis=0)
    return (grad_query, grad_key, grad_value, attended, gate_part)


def local(queries, key_proj, value_proj, grad_out, gate_vec):
    frames_local, pixels_local, clip_count, channels = queries.shape
    head_count = channels // DH
    pair_count = clip_count * head_count

    def by_pair(tensor):
        return tensor.reshape(frames_local, pixels_local, pair_count, DH)

    def by_width(tensor):
        return tensor.reshape(frames_local, pixels_local, clip_count, channels)

    space_size = lax.axis_size("space")
    pairs_local = pair_count // space_size
    stacked = jnp.stack([by_pair(queries), by_pair(key_proj), by_pair(value_proj), by_pair(grad_out)], axis=3)
    stacked = jnp.transpose(stacked, (2, 0, 1, 3, 4))
    gathered = lax.all_to_all(stacked, "space", split_axis=0, concat_axis=2, tiled=True)
    query_all, key_all, value_all, upstream_all = (
        jnp.transpose(gathered[:, :, :, part, :], (1, 2, 0, 3)) for part in range(4)
    )
    gate_rows = lax.dynamic_slice_in_dim(
        gate_vec.reshape(pair_count, DH), lax.axis_index("space") * pairs_local, pairs_local, 0
    )
    per_pair = jax.vmap(item_grads, in_axes=(1, 1, 1, 1, 0), out_axes=(1, 1, 1, 1, 0))
    per_frame = jax.vmap(per_pair, in_axes=(0, 0, 0, 0, None), out_axes=0)
    grad_query, grad_key, grad_value, attended, gate_parts = per_frame(
        query_all, key_all, value_all, upstream_all, gate_rows
    )
    grads = jnp.stack([grad_query, grad_key, grad_value], axis=3)
    grads = jnp.transpose(grads, (2, 0, 1, 3, 4))
    grads = grads.reshape(pairs_local, frames_local, space_size, pixels_local * 3, DH)
    back = lax.all_to_all(grads, "space", split_axis=2, concat_axis=0, tiled=True)
    back = back.reshape(pair_count, frames_local, pixels_local, 3, DH)
    back_query, back_key, back_value = (
        jnp.transpose(back[:, :, :, part, :], (1, 2, 0, 3)) for part in range(3)
    )
    pair_terms = jnp.sum(gate_parts, axis=0)
    grad_gate = lax.psum(pair_terms, "frame")
    return (by_width(back_query), by_width(back_key), by_width(back_value), grad_gate)


def solution(mesh):
    in_specs = (
        P("frame", "space", None, None),
        P("frame", "space", None, None),
        P("frame", "space", None, None),
        P("frame", "space", None, None),
        P(),
    )
    out_specs = (
        P("frame", "space", None, None),
        P("frame", "space", None, None),
        P("frame", "space", None, None),
        P("space", None),
    )
    return jax.shard_map(local, mesh=mesh, in_specs=in_specs, out_specs=out_specs, check_vma=False)
```

```python
import math

import jax
import jax.numpy as jnp
from jax import lax
from jax.experimental import pallas as pl
from jax.sharding import PartitionSpec as P

DH = 128


def shortened(value):

    def short(part):
        return part.astype(jnp.bfloat16) if part.dtype == jnp.float32 else part

    return jax.tree.map(short, value)


def item_grads(query_one, key_one, value_one, upstream, gate_row):
    channels = query_one.shape[1]
    inv_root = 1.0 / math.sqrt(channels)
    scores = jnp.dot(query_one, key_one.T, preferred_element_type=jnp.float32) * inv_root
    row_peak = jnp.max(scores, axis=-1, keepdims=True)
    exp_terms = jnp.exp(scores - row_peak)
    attention = exp_terms / jnp.sum(exp_terms, axis=-1, keepdims=True)
    attention_low = attention.astype(jnp.bfloat16)
    attended_blk = jnp.dot(attention_low, value_one, preferred_element_type=jnp.float32)
    upstream_wide = upstream.astype(jnp.float32)
    cotangent = (gate_row[None, :] * upstream_wide).astype(jnp.bfloat16)
    gate_part = jnp.sum(upstream_wide * attended_blk, axis=0)
    grad_attn = jnp.dot(cotangent, value_one.T, preferred_element_type=jnp.float32)
    row_terms = jnp.sum(cotangent.astype(jnp.float32) * attended_blk, axis=-1, keepdims=True)
    grad_scores = (attention * (grad_attn - row_terms)).astype(jnp.bfloat16)
    query_parts = [
        (jnp.dot(grad_scores, key_one, preferred_element_type=jnp.float32) * inv_root).astype(
            jnp.bfloat16
        )
    ]
    attended_parts = [attended_blk]
    key_acc = jnp.dot(grad_scores.T, query_one, preferred_element_type=jnp.float32)
    value_acc = jnp.dot(attention_low.T, cotangent, preferred_element_type=jnp.float32)
    grad_query = jnp.concatenate(query_parts, axis=0)
    grad_key = (key_acc * inv_root).astype(jnp.bfloat16)
    grad_value = value_acc.astype(jnp.bfloat16)
    attended = jnp.concatenate(attended_parts, axis=0)
    return (grad_query, grad_key, grad_value, attended, gate_part)


def attention_kernel(q_ref, k_ref, v_ref, up_ref, gate_ref, gq_ref, gk_ref, gv_ref, gp_ref):
    query_one = q_ref[...]
    key_one = k_ref[...]
    value_one = v_ref[...]
    inv_root = 1.0 / math.sqrt(query_one.shape[1])
    by_last = (((1,), (1,)), ((), ()))
    by_first = (((0,), (0,)), ((), ()))
    scores = lax.dot_general(query_one, key_one, by_last, preferred_element_type=jnp.float32) * inv_root
    row_peak = jnp.max(scores, axis=-1, keepdims=True)
    exp_terms = jnp.exp(scores - row_peak)
    attention = exp_terms / jnp.sum(exp_terms, axis=-1, keepdims=True)
    attention_low = attention.astype(jnp.bfloat16)
    attended = jnp.dot(attention_low, value_one, preferred_element_type=jnp.float32)
    upstream_wide = up_ref[...].astype(jnp.float32)
    cotangent = (gate_ref[...] * upstream_wide).astype(jnp.bfloat16)
    gp_ref[...] = jnp.sum(upstream_wide * attended, axis=0, keepdims=True)
    grad_attn = lax.dot_general(cotangent, value_one, by_last, preferred_element_type=jnp.float32)
    row_terms = jnp.sum(cotangent.astype(jnp.float32) * attended, axis=-1, keepdims=True)
    grad_scores = (attention * (grad_attn - row_terms)).astype(jnp.bfloat16)
    gq_ref[...] = (jnp.dot(grad_scores, key_one, preferred_element_type=jnp.float32) * inv_root).astype(
        jnp.bfloat16
    )
    gk_ref[...] = (
        lax.dot_general(grad_scores, query_one, by_first, preferred_element_type=jnp.float32) * inv_root
    ).astype(jnp.bfloat16)
    gv_ref[...] = lax.dot_general(
        attention_low, cotangent, by_first, preferred_element_type=jnp.float32
    ).astype(jnp.bfloat16)


def attention_grads(query_all, key_all, value_all, upstream_all, gate_all):
    items, rows, channels = query_all.shape
    row_block = pl.BlockSpec((None, rows, channels), lambda i: (i, 0, 0))
    gate_block = pl.BlockSpec((None, 1, channels), lambda i: (i, 0, 0))
    grad_shape = jax.ShapeDtypeStruct((items, rows, channels), jnp.bfloat16)
    return pl.pallas_call(
        attention_kernel,
        grid=(items,),
        in_specs=[row_block, row_block, row_block, row_block, gate_block],
        out_specs=[row_block, row_block, row_block, gate_block],
        out_shape=[grad_shape, grad_shape, grad_shape, jax.ShapeDtypeStruct((items, 1, channels), jnp.float32)],
    )(query_all, key_all, value_all, upstream_all, gate_all)


def local(queries, key_proj, value_proj, grad_out, gate_vec):
    frames_local, pixels_local, clip_count, channels = queries.shape
    head_count = channels // DH
    pair_count = clip_count * head_count

    def by_pair(tensor):
        return tensor.reshape(frames_local, pixels_local, pair_count, DH)

    def by_width(tensor):
        return tensor.reshape(frames_local, pixels_local, clip_count, channels)

    space_size = lax.axis_size("space")
    pairs_local = pair_count // space_size
    stacked = jnp.stack([by_pair(queries), by_pair(key_proj), by_pair(value_proj), by_pair(grad_out)], axis=3)
    stacked = jnp.transpose(stacked, (2, 0, 1, 3, 4))
    gathered = lax.all_to_all(stacked, "space", split_axis=0, concat_axis=2, tiled=True)
    items = pairs_local * frames_local
    query_all, key_all, value_all, upstream_all = (
        gathered[:, :, :, part, :].reshape(items, -1, DH) for part in range(4)
    )
    gate_rows = lax.dynamic_slice_in_dim(
        gate_vec.reshape(pair_count, DH), lax.axis_index("space") * pairs_local, pairs_local, 0
    )
    gate_all = jnp.broadcast_to(gate_rows[:, None, None, :], (pairs_local, frames_local, 1, DH))
    grad_query, grad_key, grad_value, gate_parts = attention_grads(
        query_all, key_all, value_all, upstream_all, gate_all.reshape(items, 1, DH)
    )
    grads = jnp.stack([grad_query, grad_key, grad_value], axis=2)
    grads = grads.reshape(pairs_local, frames_local, space_size, pixels_local * 3, DH)
    back = lax.all_to_all(grads, "space", split_axis=2, concat_axis=0, tiled=True)
    back = back.reshape(pair_count, frames_local, pixels_local, 3, DH)
    back_query, back_key, back_value = (
        jnp.transpose(back[:, :, :, part, :], (1, 2, 0, 3)) for part in range(3)
    )
    pair_terms = jnp.sum(gate_parts.reshape(pairs_local, frames_local, DH), axis=1)
    grad_gate = lax.psum(pair_terms, "frame")
    return (by_width(back_query), by_width(back_key), by_width(back_value), grad_gate)


def solution(mesh):
    in_specs = (
        P("frame", "space", None, None),
        P("frame", "space", None, None),
        P("frame", "space", None, None),
        P("frame", "space", None, None),
        P(),
    )
    out_specs = (
        P("frame", "space", None, None),
        P("frame", "space", None, None),
        P("frame", "space", None, None),
        P("space", None),
    )
    return jax.shard_map(local, mesh=mesh, in_specs=in_specs, out_specs=out_specs, check_vma=False)
```

```python
import math

import jax
import jax.numpy as jnp
from jax import lax
from jax.sharding import PartitionSpec as P

DH = 128


def shortened(value):

    def short(part):
        return part.astype(jnp.bfloat16) if part.dtype == jnp.float32 else part

    return jax.tree.map(short, value)


def item_grads(query_one, key_one, value_one, upstream, gate_row):
    channels = query_one.shape[1]
    inv_root = 1.0 / math.sqrt(channels)
    scores = jnp.dot(query_one, key_one.T, preferred_element_type=jnp.float32) * inv_root
    row_peak = jnp.max(scores, axis=-1, keepdims=True)
    exp_terms = jnp.exp(scores - row_peak)
    attention = exp_terms / jnp.sum(exp_terms, axis=-1, keepdims=True)
    attention_low = attention.astype(jnp.bfloat16)
    attended_blk = jnp.dot(attention_low, value_one, preferred_element_type=jnp.float32)
    upstream_wide = upstream.astype(jnp.float32)
    cotangent = (gate_row[None, :] * upstream_wide).astype(jnp.bfloat16)
    gate_part = jnp.sum(upstream_wide * attended_blk, axis=0)
    grad_attn = jnp.dot(cotangent, value_one.T, preferred_element_type=jnp.float32)
    row_terms = jnp.sum(cotangent.astype(jnp.float32) * attended_blk, axis=-1, keepdims=True)
    grad_scores = (attention * (grad_attn - row_terms)).astype(jnp.bfloat16)
    query_parts = [
        (jnp.dot(grad_scores, key_one, preferred_element_type=jnp.float32) * inv_root).astype(
            jnp.bfloat16
        )
    ]
    attended_parts = [attended_blk]
    key_acc = jnp.dot(grad_scores.T, query_one, preferred_element_type=jnp.float32)
    value_acc = jnp.dot(attention_low.T, cotangent, preferred_element_type=jnp.float32)
    grad_query = jnp.concatenate(query_parts, axis=0)
    grad_key = (key_acc * inv_root).astype(jnp.bfloat16)
    grad_value = value_acc.astype(jnp.bfloat16)
    attended = jnp.concatenate(attended_parts, axis=0)
    return (grad_query, grad_key, grad_value, attended, gate_part)


def local(queries, key_proj, value_proj, grad_out, gate_vec):
    frames_local, pixels_local, clip_count, channels = queries.shape
    head_count = channels // DH
    pair_count = clip_count * head_count

    def by_pair(tensor):
        return tensor.reshape(frames_local, pixels_local, pair_count, DH)

    def by_width(tensor):
        return tensor.reshape(frames_local, pixels_local, clip_count, channels)

    space_size = lax.axis_size("space")
    pairs_local = pair_count // space_size
    stacked = jnp.concatenate(
        [by_pair(t) for t in (queries, key_proj, value_proj, grad_out)], axis=3
    )
    stacked = jnp.transpose(stacked, (2, 0, 1, 3))
    gathered = lax.all_to_all(stacked, "space", split_axis=0, concat_axis=2, tiled=True)
    query_all, key_all, value_all, upstream_all = (
        jnp.transpose(gathered[:, :, :, part * DH:(part + 1) * DH], (1, 2, 0, 3)) for part in range(4)
    )
    gate_rows = lax.dynamic_slice_in_dim(
        gate_vec.reshape(pair_count, DH), lax.axis_index("space") * pairs_local, pairs_local, 0
    )
    per_pair = jax.vmap(item_grads, in_axes=(1, 1, 1, 1, 0), out_axes=(1, 1, 1, 1, 0))
    per_frame = jax.vmap(per_pair, in_axes=(0, 0, 0, 0, None), out_axes=0)
    grad_query, grad_key, grad_value, attended, gate_parts = per_frame(
        query_all, key_all, value_all, upstream_all, gate_rows
    )
    grads = jnp.stack([grad_query, grad_key, grad_value], axis=0)
    grads = grads.reshape(3, frames_local, space_size, pixels_local, pairs_local, DH)
    grads = jnp.transpose(grads, (4, 1, 2, 0, 3, 5))
    back = lax.all_to_all(grads, "space", split_axis=2, concat_axis=0, tiled=True)
    back_query, back_key, back_value = (
        jnp.transpose(back[:, :, 0, part], (1, 2, 0, 3)) for part in range(3)
    )
    pair_terms = jnp.sum(gate_parts, axis=0)
    grad_gate = lax.psum(pair_terms, "frame")
    return (by_width(back_query), by_width(back_key), by_width(back_value), grad_gate)


def solution(mesh):
    in_specs = (
        P("frame", "space", None, None),
        P("frame", "space", None, None),
        P("frame", "space", None, None),
        P("frame", "space", None, None),
        P(),
    )
    out_specs = (
        P("frame", "space", None, None),
        P("frame", "space", None, None),
        P("frame", "space", None, None),
        P("space", None),
    )
    return jax.shard_map(local, mesh=mesh, in_specs=in_specs, out_specs=out_specs, check_vma=False)
```

```python
import math

import jax
import jax.numpy as jnp
from jax import lax
from jax.sharding import PartitionSpec as P

DH = 128


def shortened(value):

    def short(part):
        return part.astype(jnp.bfloat16) if part.dtype == jnp.float32 else part

    return jax.tree.map(short, value)


def item_grads(query_one, key_one, value_one, upstream, gate_row):
    channels = query_one.shape[1]
    inv_root = 1.0 / math.sqrt(channels)
    scores = jnp.dot(query_one, key_one.T, preferred_element_type=jnp.float32) * inv_root
    row_peak = jnp.max(scores, axis=-1, keepdims=True)
    exp_terms = jnp.exp(scores - row_peak)
    attention = exp_terms / jnp.sum(exp_terms, axis=-1, keepdims=True)
    attention_low = attention.astype(jnp.bfloat16)
    attended_blk = jnp.dot(attention_low, value_one, preferred_element_type=jnp.float32)
    upstream_wide = upstream.astype(jnp.float32)
    cotangent = (gate_row[None, :] * upstream_wide).astype(jnp.bfloat16)
    gate_part = jnp.sum(upstream_wide * attended_blk, axis=0)
    grad_attn = jnp.dot(cotangent, value_one.T, preferred_element_type=jnp.float32)
    row_terms = jnp.sum(cotangent.astype(jnp.float32) * attended_blk, axis=-1, keepdims=True)
    grad_scores = (attention * (grad_attn - row_terms)).astype(jnp.bfloat16)
    query_parts = [
        (jnp.dot(grad_scores, key_one, preferred_element_type=jnp.float32) * inv_root).astype(
            jnp.bfloat16
        )
    ]
    attended_parts = [attended_blk]
    key_acc = jnp.dot(grad_scores.T, query_one, preferred_element_type=jnp.float32)
    value_acc = jnp.dot(attention_low.T, cotangent, preferred_element_type=jnp.float32)
    grad_query = jnp.concatenate(query_parts, axis=0)
    grad_key = (key_acc * inv_root).astype(jnp.bfloat16)
    grad_value = value_acc.astype(jnp.bfloat16)
    attended = jnp.concatenate(attended_parts, axis=0)
    return (grad_query, grad_key, grad_value, attended, gate_part)


def local(queries, key_proj, value_proj, grad_out, gate_vec):
    frames_local, pixels_local, clip_count, channels = queries.shape
    head_count = channels // DH
    pair_count = clip_count * head_count

    def by_pair(tensor):
        return tensor.reshape(frames_local, pixels_local, pair_count, DH)

    def by_width(tensor):
        return tensor.reshape(frames_local, pixels_local, clip_count, channels)

    space_size = lax.axis_size("space")
    pairs_local = pair_count // space_size
    joined = jnp.concatenate([queries, key_proj, value_proj, grad_out], axis=3)
    joined = joined.reshape(frames_local, pixels_local, clip_count, 4, head_count, DH)
    picker = jnp.eye(clip_count, dtype=joined.dtype)
    stacked = jnp.einsum("fibahd,bc->chfiad", joined, picker, preferred_element_type=jnp.float32)
    stacked = stacked.astype(joined.dtype).reshape(pair_count, frames_local, pixels_local, 4 * DH)
    gathered = lax.all_to_all(stacked, "space", split_axis=0, concat_axis=2, tiled=True)
    query_all, key_all, value_all, upstream_all = (
        jnp.transpose(gathered[:, :, :, part * DH:(part + 1) * DH], (1, 2, 0, 3)) for part in range(4)
    )
    gate_rows = lax.dynamic_slice_in_dim(
        gate_vec.reshape(pair_count, DH), lax.axis_index("space") * pairs_local, pairs_local, 0
    )
    per_pair = jax.vmap(item_grads, in_axes=(1, 1, 1, 1, 0), out_axes=(1, 1, 1, 1, 0))
    per_frame = jax.vmap(per_pair, in_axes=(0, 0, 0, 0, None), out_axes=0)
    grad_query, grad_key, grad_value, attended, gate_parts = per_frame(
        query_all, key_all, value_all, upstream_all, gate_rows
    )
    grads = jnp.stack([grad_query, grad_key, grad_value], axis=0)
    grads = grads.reshape(3, frames_local, space_size, pixels_local, pairs_local, DH)
    grads = jnp.transpose(grads, (4, 1, 2, 0, 3, 5))
    back = lax.all_to_all(grads, "space", split_axis=2, concat_axis=0, tiled=True)
    back_query, back_key, back_value = (
        jnp.transpose(back[:, :, 0, part], (1, 2, 0, 3)) for part in range(3)
    )
    pair_terms = jnp.sum(gate_parts, axis=0)
    grad_gate = lax.psum(pair_terms, "frame")
    return (by_width(back_query), by_width(back_key), by_width(back_value), grad_gate)


def solution(mesh):
    in_specs = (
        P("frame", "space", None, None),
        P("frame", "space", None, None),
        P("frame", "space", None, None),
        P("frame", "space", None, None),
        P(),
    )
    out_specs = (
        P("frame", "space", None, None),
        P("frame", "space", None, None),
        P("frame", "space", None, None),
        P("space", None),
    )
    return jax.shard_map(local, mesh=mesh, in_specs=in_specs, out_specs=out_specs, check_vma=False)
```

```python
import math

import jax
import jax.numpy as jnp
from jax import lax
from jax.sharding import PartitionSpec as P

DH = 128


def shortened(value):

    def short(part):
        return part.astype(jnp.bfloat16) if part.dtype == jnp.float32 else part

    return jax.tree.map(short, value)


def item_grads(query_one, key_one, value_one, upstream, gate_row):
    channels = query_one.shape[1]
    inv_root = 1.0 / math.sqrt(channels)
    scores = jnp.dot(query_one, key_one.T, preferred_element_type=jnp.float32) * inv_root
    row_peak = jnp.max(scores, axis=-1, keepdims=True)
    exp_terms = jnp.exp(scores - row_peak)
    attention = exp_terms / jnp.sum(exp_terms, axis=-1, keepdims=True)
    attention_low = attention.astype(jnp.bfloat16)
    attended_blk = jnp.dot(attention_low, value_one, preferred_element_type=jnp.float32)
    upstream_wide = upstream.astype(jnp.float32)
    cotangent = (gate_row[None, :] * upstream_wide).astype(jnp.bfloat16)
    gate_part = jnp.sum(upstream_wide * attended_blk, axis=0)
    grad_attn = jnp.dot(cotangent, value_one.T, preferred_element_type=jnp.float32)
    row_terms = jnp.sum(cotangent.astype(jnp.float32) * attended_blk, axis=-1, keepdims=True)
    grad_scores = (attention * (grad_attn - row_terms)).astype(jnp.bfloat16)
    query_parts = [
        (jnp.dot(grad_scores, key_one, preferred_element_type=jnp.float32) * inv_root).astype(
            jnp.bfloat16
        )
    ]
    attended_parts = [attended_blk]
    key_acc = jnp.dot(grad_scores.T, query_one, preferred_element_type=jnp.float32)
    value_acc = jnp.dot(attention_low.T, cotangent, preferred_element_type=jnp.float32)
    grad_query = jnp.concatenate(query_parts, axis=0)
    grad_key = (key_acc * inv_root).astype(jnp.bfloat16)
    grad_value = value_acc.astype(jnp.bfloat16)
    attended = jnp.concatenate(attended_parts, axis=0)
    return (grad_query, grad_key, grad_value, attended, gate_part)


def local(queries, key_proj, value_proj, grad_out, gate_vec):
    frames_local, pixels_local, clip_count, channels = queries.shape
    head_count = channels // DH
    pair_count = clip_count * head_count

    def by_pair(tensor):
        return tensor.reshape(frames_local, pixels_local, pair_count, DH)

    def by_width(tensor):
        return tensor.reshape(frames_local, pixels_local, clip_count, channels)

    space_size = lax.axis_size("space")
    pairs_local = pair_count // space_size
    joined = jnp.concatenate([queries, key_proj, value_proj, grad_out], axis=3)
    joined = joined.reshape(frames_local, pixels_local, clip_count, 4, head_count, DH)
    picker = jnp.eye(clip_count, dtype=joined.dtype)
    stacked = jnp.einsum("fibahd,bc->chfiad", joined, picker, preferred_element_type=jnp.float32)
    stacked = stacked.astype(joined.dtype).reshape(pair_count, frames_local, pixels_local, 4, DH)
    gathered = lax.all_to_all(stacked, "space", split_axis=0, concat_axis=2, tiled=True)
    query_all, key_all, value_all, upstream_all = (
        jnp.transpose(gathered[:, :, :, part, :], (1, 2, 0, 3)) for part in range(4)
    )
    gate_rows = lax.dynamic_slice_in_dim(
        gate_vec.reshape(pair_count, DH), lax.axis_index("space") * pairs_local, pairs_local, 0
    )
    per_pair = jax.vmap(item_grads, in_axes=(1, 1, 1, 1, 0), out_axes=(1, 1, 1, 1, 0))
    per_frame = jax.vmap(per_pair, in_axes=(0, 0, 0, 0, None), out_axes=0)
    grad_query, grad_key, grad_value, attended, gate_parts = per_frame(
        query_all, key_all, value_all, upstream_all, gate_rows
    )
    grads = jnp.stack([grad_query, grad_key, grad_value], axis=0)
    grads = grads.reshape(3, frames_local, space_size, pixels_local, pairs_local, DH)
    grads = jnp.transpose(grads, (4, 1, 2, 0, 3, 5))
    back = lax.all_to_all(grads, "space", split_axis=2, concat_axis=0, tiled=True)
    back_query, back_key, back_value = (
        jnp.transpose(back[:, :, 0, part], (1, 2, 0, 3)) for part in range(3)
    )
    pair_terms = jnp.sum(gate_parts, axis=0)
    grad_gate = lax.psum(pair_terms, "frame")
    return (by_width(back_query), by_width(back_key), by_width(back_value), grad_gate)


def solution(mesh):
    in_specs = (
        P("frame", "space", None, None),
        P("frame", "space", None, None),
        P("frame", "space", None, None),
        P("frame", "space", None, None),
        P(),
    )
    out_specs = (
        P("frame", "space", None, None),
        P("frame", "space", None, None),
        P("frame", "space", None, None),
        P("space", None),
    )
    return jax.shard_map(local, mesh=mesh, in_specs=in_specs, out_specs=out_specs, check_vma=False)
```

```python
import math

import jax
import jax.numpy as jnp
from jax import lax
from jax.sharding import PartitionSpec as P

DH = 128


def shortened(value):

    def short(part):
        return part.astype(jnp.bfloat16) if part.dtype == jnp.float32 else part

    return jax.tree.map(short, value)


def item_grads(query_one, key_one, value_one, upstream, gate_row):
    channels = query_one.shape[1]
    inv_root = 1.0 / math.sqrt(channels)
    scores = jnp.dot(query_one, key_one.T, preferred_element_type=jnp.float32) * inv_root
    row_peak = jnp.max(scores, axis=-1, keepdims=True)
    exp_terms = jnp.exp(scores - row_peak)
    attention = exp_terms / jnp.sum(exp_terms, axis=-1, keepdims=True)
    attention_low = attention.astype(jnp.bfloat16)
    attended_blk = jnp.dot(attention_low, value_one, preferred_element_type=jnp.float32)
    upstream_wide = upstream.astype(jnp.float32)
    cotangent = (gate_row[None, :] * upstream_wide).astype(jnp.bfloat16)
    gate_part = jnp.sum(upstream_wide * attended_blk, axis=0)
    grad_attn = jnp.dot(cotangent, value_one.T, preferred_element_type=jnp.float32)
    row_terms = jnp.sum(cotangent.astype(jnp.float32) * attended_blk, axis=-1, keepdims=True)
    grad_scores = (attention * (grad_attn - row_terms)).astype(jnp.bfloat16)
    query_parts = [
        (jnp.dot(grad_scores, key_one, preferred_element_type=jnp.float32) * inv_root).astype(
            jnp.bfloat16
        )
    ]
    attended_parts = [attended_blk]
    key_acc = jnp.dot(grad_scores.T, query_one, preferred_element_type=jnp.float32)
    value_acc = jnp.dot(attention_low.T, cotangent, preferred_element_type=jnp.float32)
    grad_query = jnp.concatenate(query_parts, axis=0)
    grad_key = (key_acc * inv_root).astype(jnp.bfloat16)
    grad_value = value_acc.astype(jnp.bfloat16)
    attended = jnp.concatenate(attended_parts, axis=0)
    return (grad_query, grad_key, grad_value, attended, gate_part)


def local(queries, key_proj, value_proj, grad_out, gate_vec):
    frames_local, pixels_local, clip_count, channels = queries.shape
    head_count = channels // DH
    pair_count = clip_count * head_count

    def by_pair(tensor):
        return tensor.reshape(frames_local, pixels_local, pair_count, DH)

    def by_width(tensor):
        return tensor.reshape(frames_local, pixels_local, clip_count, channels)

    space_size = lax.axis_size("space")
    pairs_local = pair_count // space_size
    joined = jnp.concatenate([queries, key_proj, value_proj, grad_out], axis=3)
    joined = joined.reshape(frames_local, pixels_local, clip_count, 4, head_count, DH)
    picker = jnp.eye(clip_count, dtype=joined.dtype)
    stacked = jnp.einsum("fibahd,bc->chfiad", joined, picker, preferred_element_type=jnp.float32)
    stacked = stacked.astype(joined.dtype).reshape(pair_count, frames_local, pixels_local, 4, DH)
    gathered = lax.all_to_all(stacked, "space", split_axis=0, concat_axis=2, tiled=True)
    splitter = jnp.eye(4, dtype=gathered.dtype)
    split_all = jnp.einsum("pfrad,ac->cfrpd", gathered, splitter, preferred_element_type=jnp.float32)
    split_all = split_all.astype(gathered.dtype)
    query_all, key_all, value_all, upstream_all = (split_all[part] for part in range(4))
    gate_rows = lax.dynamic_slice_in_dim(
        gate_vec.reshape(pair_count, DH), lax.axis_index("space") * pairs_local, pairs_local, 0
    )
    per_pair = jax.vmap(item_grads, in_axes=(1, 1, 1, 1, 0), out_axes=(1, 1, 1, 1, 0))
    per_frame = jax.vmap(per_pair, in_axes=(0, 0, 0, 0, None), out_axes=0)
    grad_query, grad_key, grad_value, attended, gate_parts = per_frame(
        query_all, key_all, value_all, upstream_all, gate_rows
    )
    grads = jnp.stack([grad_query, grad_key, grad_value], axis=0)
    grads = grads.reshape(3, frames_local, space_size, pixels_local, pairs_local, DH)
    grads = jnp.transpose(grads, (4, 1, 2, 0, 3, 5))
    back = lax.all_to_all(grads, "space", split_axis=2, concat_axis=0, tiled=True)
    back_query, back_key, back_value = (
        jnp.transpose(back[:, :, 0, part], (1, 2, 0, 3)) for part in range(3)
    )
    pair_terms = jnp.sum(gate_parts, axis=0)
    grad_gate = lax.psum(pair_terms, "frame")
    return (by_width(back_query), by_width(back_key), by_width(back_value), grad_gate)


def solution(mesh):
    in_specs = (
        P("frame", "space", None, None),
        P("frame", "space", None, None),
        P("frame", "space", None, None),
        P("frame", "space", None, None),
        P(),
    )
    out_specs = (
        P("frame", "space", None, None),
        P("frame", "space", None, None),
        P("frame", "space", None, None),
        P("space", None),
    )
    return jax.shard_map(local, mesh=mesh, in_specs=in_specs, out_specs=out_specs, check_vma=False)
```
